32 devices in a mesh: grp: 2 (over x), row: 8 (over z, y), col: 2 (over core).
Axes of the slice: x: 2, y: 2, z: 4, core: 2. Of those that a mesh axis runs over, the one named last changes fastest.
Arguments:
- green: float32 [4, 256, 256, 256], P('grp', None, 'row', 'col'), parts along dimension 0, may hold values from -6 to 6
- hamiltonian: float32 [4, 256, 256], P('grp'), parts along dimension 0
- onebody: float32 [4, 256, 256], P('grp'), parts along dimension 0, may hold values from -5 to 5
- site_map: int32 [256], replicated, may hold values from 0 to 31
- onsite_u: float32 [32], replicated, may hold values from 0.5 to 2
- pair_first: int32 [4096], replicated, may hold values from 0 to 255
- pair_second: int32 [4096], replicated, may hold values from 0 to 255
Outputs:
- advanced: float32 [4, 256, 256, 256], P('grp', None, 'row', 'col'), parts along dimension 0
The draws below stay inside these ranges and needn't reach their ends.
There are 2 independent parts, one for each index of `grp`. The reference program is written for one: setup_inputs(seed, part) draws one part's arguments, and reference() takes and returns one part's arrays. A program takes and returns all parts, laid end to end along the dimension named above; an argument that names none is the same for every part. Nothing has to cross between parts.
All inputs are finite; a program needn't handle non-finite values.
Results may differ from the reference program's by a relative error of at most 0.00005.
Values sent between devices are 32-bit elements; how exact they have to be, the bound alone decides.
No kernel may reach another device: no remote copies, remote signals or barrier semaphores. Data moves between devices by JAX's collectives and lax.ppermute only.
A program may use at most 192 MiB of HBM per device.

```python
import math
import jax
import jax.numpy as jnp
from jax import lax

ORB = 256
NSITE = 32
NPAIR = 4096


def draw_hamiltonian(key, part):
    raw = jax.random.normal(key, (2, ORB, ORB), jnp.float32)
    scale = (2.0 * ORB) ** (-0.5)
    real_part = (raw[0] + raw[0].T) * scale
    imag_part = (raw[1] - raw[1].T) * scale
    return jnp.stack([real_part, imag_part]).astype(jnp.float32)


def set_ends(entries, rng, least, largest):
    longest = entries.shape.index(max(entries.shape))
    spots = []
    for shift in (0, 1):
        where = [jax.random.randint(jax.random.fold_in(rng, axis), (), 0, length) for axis, length in enumerate(entries.shape)]
        where[longest] = (where[longest] + shift) % entries.shape[longest]
        spots.append(tuple(where))
    return entries.at[spots[0]].set(least).at[spots[1]].set(largest)


def steps_of(own_key, extent, cuts, least, high):
    factor_of, own = 1.0, jax.random.fold_in(own_key, 6)
    for position, parts in cuts:
        steps = jnp.exp(jax.random.uniform(jax.random.fold_in(own, position), (parts,), jnp.float32, least / len(cuts), high / len(cuts)))
        factor_of = factor_of * jnp.repeat(steps, extent[position] // parts).reshape([-1 if axis == position else 1 for axis in range(len(extent))])
    return factor_of


def noise(stream_key, extent, deviation, bound, shards=(), kind=jnp.bfloat16):
    drawn = deviation * jax.random.normal(stream_key, extent, jnp.float32)
    if shards:
        drawn = drawn * steps_of(stream_key, extent, shards, -0.22, 0.18)
    return jnp.clip(drawn, -bound, bound).astype(kind)


def setup_inputs(seed: int = 0, part: int = 0) -> dict:
    keys = jax.random.split(jax.random.key(seed), 8)
    part_keys = jax.random.split(jax.random.fold_in(keys[7], part), 8)
    green = noise(part_keys[0], (2, ORB, ORB, ORB), 1.0, 6.0, ((2, 8), (3, 2)), jnp.float32)
    hamiltonian = draw_hamiltonian(jax.random.fold_in(jax.random.fold_in(keys[7], part), 71), part)
    onebody = noise(part_keys[2], (2, ORB, ORB), 0.8, 5.0, (), jnp.float32)
    site_map = set_ends(jax.random.randint(keys[3], (ORB,), 0, NSITE), jax.random.fold_in(keys[3], 1), 0, NSITE - 1).astype(jnp.int32)
    onsite_u = jnp.clip(jnp.exp(jax.random.uniform(keys[4], (NSITE,), jnp.float32, math.log(0.5), math.log(2.0))), 0.5, 2.0)
    pair_first = set_ends(jax.random.randint(keys[5], (NPAIR,), 0, ORB), jax.random.fold_in(keys[5], 1), 0, ORB - 1).astype(jnp.int32)
    pair_second = set_ends(jax.random.randint(keys[6], (NPAIR,), 0, ORB), jax.random.fold_in(keys[6], 1), 0, ORB - 1).astype(jnp.int32)
    return {"green": green, "hamiltonian": hamiltonian, "onebody": onebody, "site_map": site_map, "onsite_u": onsite_u, "pair_first": pair_first, "pair_second": pair_second}


time_step = 0.1
highest = lax.Precision.HIGHEST


def complex_terms(hamiltonian, field):
    orbs = field.shape[1]
    hre = hamiltonian[0]
    him = hamiltonian[1]
    flat_re = field[0].reshape(orbs, -1)
    flat_im = field[1].reshape(orbs, -1)
    k_re = jnp.dot(hre, flat_re, precision=highest) - jnp.dot(him, flat_im, precision=highest)
    k_im = jnp.dot(hre, flat_im, precision=highest) + jnp.dot(him, flat_re, precision=highest)
    k_re = k_re.reshape(field[0].shape)
    k_im = k_im.reshape(field[0].shape)
    i_re = jnp.einsum("ia,kaj->kij", hre, field[0], precision=highest) - jnp.einsum("ia,kaj->kij", him, field[1], precision=highest)
    i_im = jnp.einsum("ia,kaj->kij", hre, field[1], precision=highest) + jnp.einsum("ia,kaj->kij", him, field[0], precision=highest)
    j_re = jnp.einsum("ja,kia->kij", hre, field[0], precision=highest) - jnp.einsum("ja,kia->kij", him, field[1], precision=highest)
    j_im = jnp.einsum("ja,kia->kij", hre, field[1], precision=highest) + jnp.einsum("ja,kia->kij", him, field[0], precision=highest)
    return k_re + i_re + j_re, k_im + i_im + j_im


def reference(green, hamiltonian, onebody, site_map, onsite_u, pair_first, pair_second):
    orbs = green.shape[1]
    u_rows = onsite_u[site_map]
    ladder = u_rows[:, None] * (site_map[:, None] == site_map[None, :]).astype(jnp.float32)
    levels = jnp.arange(orbs, dtype=jnp.int32)
    first_hot = (pair_first[:, None] == levels[None, :]).astype(jnp.float32)
    second_hot = (pair_second[:, None] == levels[None, :]).astype(jnp.float32)
    counts = jnp.einsum("pi,pj->ij", first_hot, second_hot, precision=highest)
    pauli = u_rows[:, None] * counts
    left = onebody
    source_re = pauli * (left[0][:, :, None] * left[0][:, None, :] - left[1][:, :, None] * left[1][:, None, :])
    source_im = pauli * (left[0][:, :, None] * left[1][:, None, :] + left[1][:, :, None] * left[0][:, None, :])

    def force(field):
        hop_re, hop_im = complex_terms(hamiltonian, field)
        total_re = hop_re + ladder * field[0] + source_re
        total_im = hop_im + ladder * field[1] + source_im
        return jnp.stack([total_im, -total_re])

    half = green + (0.5 * time_step) * force(green)
    return green + time_step * force(half)
```

```python
import jax
import jax.numpy as jnp
from jax import lax
from jax.sharding import PartitionSpec as P

time_step = 0.1
highest = lax.Precision.HIGHEST


def dot(a, b):
    return jnp.dot(a, b, precision=highest)


def neg_i(x, scale):
    return jnp.stack([scale * x[1], -scale * x[0]])


def make_on_device(nrow):
    def on_device(green, hamiltonian, onebody, site_map, onsite_u, pair_first, pair_second):
        orbs = green.shape[1]
        nrows = green.shape[2]
        ncols = green.shape[3]
        jb = ncols // nrow
        r = lax.axis_index("row")
        c = lax.axis_index("col")
        row_start = r * nrows
        col_start = c * ncols
        sub_start = col_start + r * jb
        levels = jnp.arange(onsite_u.shape[0], dtype=jnp.int32)
        orb_ids = jnp.arange(orbs, dtype=jnp.int32)
        u_all = jnp.sum(jnp.where(site_map[:, None] == levels[None, :], onsite_u[None, :], 0.0), axis=1)
        first_hot = (pair_first[:, None] == orb_ids[None, :]).astype(jnp.float32)
        second_hot = (pair_second[:, None] == orb_ids[None, :]).astype(jnp.float32)
        hre = hamiltonian[0]
        him = hamiltonian[1]

        sites_i = lax.dynamic_slice_in_dim(site_map, row_start, nrows)
        sites_j = lax.dynamic_slice_in_dim(site_map, col_start, ncols)
        u_i = lax.dynamic_slice_in_dim(u_all, row_start, nrows)
        lad_a = u_i[:, None] * (sites_i[:, None] == sites_j[None, :]).astype(jnp.float32)
        fh_a = lax.dynamic_slice_in_dim(first_hot, row_start, nrows, 1)
        sh_a = lax.dynamic_slice_in_dim(second_hot, col_start, ncols, 1)
        pauli_a = u_i[:, None] * jnp.einsum("pi,pj->ij", fh_a, sh_a, precision=highest)
        left = lax.dynamic_slice_in_dim(onebody, row_start, nrows, 2)
        right = lax.dynamic_slice_in_dim(onebody, col_start, ncols, 2)
        src_a = jnp.stack([
            pauli_a * (left[0][:, :, None] * right[0][:, None, :] - left[1][:, :, None] * right[1][:, None, :]),
            pauli_a * (left[0][:, :, None] * right[1][:, None, :] + left[1][:, :, None] * right[0][:, None, :]),
        ])

        sites_s = lax.dynamic_slice_in_dim(site_map, sub_start, jb)
        lad_b = u_all[None, :] * (sites_s[:, None] == site_map[None, :]).astype(jnp.float32)
        sh_b = lax.dynamic_slice_in_dim(second_hot, sub_start, jb, 1)
        pauli_b = u_all[None, :] * jnp.einsum("pj,pi->ji", sh_b, first_hot, precision=highest)
        g_s = lax.dynamic_slice_in_dim(onebody, sub_start, jb, 2)
        g_all = onebody
        src_b = jnp.stack([
            pauli_b * (g_s[0][:, :, None] * g_all[0][:, None, :] - g_s[1][:, :, None] * g_all[1][:, None, :]),
            pauli_b * (g_s[1][:, :, None] * g_all[0][:, None, :] + g_s[0][:, :, None] * g_all[1][:, None, :]),
        ])

        h_own = lax.dynamic_slice_in_dim(hamiltonian, col_start, ncols, 1)
        hre_own_t = h_own[0].T
        him_own_t = h_own[1].T

        def apply_j(x):
            full = lax.all_gather(x, "col", axis=3, tiled=True)
            fr = full[0].reshape(orbs * nrows, orbs)
            fi = full[1].reshape(orbs * nrows, orbs)
            out_re = dot(fr, hre_own_t) - dot(fi, him_own_t)
            out_im = dot(fi, hre_own_t) + dot(fr, him_own_t)
            return jnp.stack([out_re, out_im]).reshape(2, orbs, nrows, ncols)

        def apply_ki(x):
            xr = x[0]
            xi = x[1]
            kr = xr.reshape(orbs, jb * orbs)
            ki = xi.reshape(orbs, jb * orbs)
            k_re = (dot(hre, kr) - dot(him, ki)).reshape(orbs, jb, orbs)
            k_im = (dot(hre, ki) + dot(him, kr)).reshape(orbs, jb, orbs)
            ir = xr.reshape(orbs * jb, orbs)
            ii = xi.reshape(orbs * jb, orbs)
            i_re = (dot(ir, hre.T) - dot(ii, him.T)).reshape(orbs, jb, orbs)
            i_im = (dot(ii, hre.T) + dot(ir, him.T)).reshape(orbs, jb, orbs)
            return jnp.stack([k_re + i_re, k_im + i_im])

        def to_split(x):
            send = x.reshape(2, orbs, nrows, nrow, jb).transpose(3, 0, 1, 4, 2)
            send = send.reshape(nrow, 2, orbs, jb * nrows)
            got = lax.all_to_all(send, "row", 0, 0, tiled=True)
            got = got.reshape(nrow, 2, orbs, jb, nrows).transpose(1, 2, 3, 0, 4)
            return got.reshape(2, orbs, jb, nrow * nrows)

        def from_split(y):
            send = y.reshape(2, orbs, jb, nrow, nrows).transpose(3, 0, 1, 2, 4)
            send = send.reshape(nrow, 2, orbs, jb * nrows)
            got = lax.all_to_all(send, "row", 0, 0, tiled=True)
            got = got.reshape(nrow, 2, orbs, jb, nrows).transpose(1, 2, 4, 0, 3)
            return got.reshape(2, orbs, nrows, ncols)

        dt = time_step
        dt2 = 0.5 * time_step * time_step
        g = green
        g_b = to_split(g)
        p = apply_j(g)
        p_b = to_split(p)
        q = apply_ki(g_b) + lad_b * g_b
        e = p_b + q + src_b
        w = e + p_b
        part_b = neg_i(q, dt) - dt2 * (apply_ki(w) + lad_b * e)
        part_b_a = from_split(part_b)
        e2 = p + lad_a * g + src_a
        part_a = g + neg_i(p + src_a, dt) - dt2 * apply_j(e2)
        return part_a + part_b_a

    return on_device


def solution(mesh):
    placed = (
        P("grp", None, "row", "col"),
        P("grp", None, None),
        P("grp", None, None),
        P(),
        P(),
        P(),
        P(),
    )
    return jax.shard_map(
        make_on_device(mesh.shape["row"]),
        mesh=mesh,
        in_specs=placed,
        out_specs=P("grp", None, "row", "col"),
        check_vma=False,
    )
```

```python
import jax
import jax.numpy as jnp
from jax import lax
from jax.sharding import PartitionSpec as P

time_step = 0.1
highest = lax.Precision.HIGHEST


def neg_i(x, scale):
    return jnp.stack([scale * x[1], -scale * x[0]])


def make_on_device(nrow, ncol):
    ndev = nrow * ncol

    def on_device(green, hamiltonian, onebody, site_map, onsite_u, pair_first, pair_second):
        orbs = green.shape[1]
        nrows = green.shape[2]
        ncols = green.shape[3]
        kb = orbs // ndev
        r = lax.axis_index("row")
        c = lax.axis_index("col")
        row_start = r * nrows
        col_start = c * ncols
        k_start = (r * ncol + c) * kb
        levels = jnp.arange(onsite_u.shape[0], dtype=jnp.int32)
        orb_ids = jnp.arange(orbs, dtype=jnp.int32)
        u_all = jnp.sum(jnp.where(site_map[:, None] == levels[None, :], onsite_u[None, :], 0.0), axis=1)
        first_hot = (pair_first[:, None] == orb_ids[None, :]).astype(jnp.float32)
        second_hot = (pair_second[:, None] == orb_ids[None, :]).astype(jnp.float32)
        hre = hamiltonian[0]
        him = hamiltonian[1]
        h_big = jnp.concatenate(
            [jnp.concatenate([hre, -him], axis=1), jnp.concatenate([him, hre], axis=1)], axis=0
        )
        hre_t = hre.T
        him_t = him.T

        sites_i = lax.dynamic_slice_in_dim(site_map, row_start, nrows)
        sites_j = lax.dynamic_slice_in_dim(site_map, col_start, ncols)
        u_i = lax.dynamic_slice_in_dim(u_all, row_start, nrows)
        lad_a = u_i[:, None] * (sites_i[:, None] == sites_j[None, :]).astype(jnp.float32)
        fh_a = lax.dynamic_slice_in_dim(first_hot, row_start, nrows, 1)
        sh_a = lax.dynamic_slice_in_dim(second_hot, col_start, ncols, 1)
        pauli_a = u_i[:, None] * jnp.einsum("pi,pj->ij", fh_a, sh_a, precision=highest)
        left = lax.dynamic_slice_in_dim(onebody, row_start, nrows, 2)
        right = lax.dynamic_slice_in_dim(onebody, col_start, ncols, 2)
        src_a = jnp.stack([
            pauli_a * (left[0][:, :, None] * right[0][:, None, :] - left[1][:, :, None] * right[1][:, None, :]),
            pauli_a * (left[0][:, :, None] * right[1][:, None, :] + left[1][:, :, None] * right[0][:, None, :]),
        ])

        lad_k = u_all[:, None] * (site_map[:, None] == site_map[None, :]).astype(jnp.float32)
        pauli_k = u_all[:, None] * jnp.einsum("pi,pj->ij", first_hot, second_hot, precision=highest)
        gk = lax.dynamic_slice_in_dim(onebody, k_start, kb, 1)
        gi_r = gk[0].T[:, :, None]
        gi_i = gk[1].T[:, :, None]
        gj_r = gk[0][None, :, :]
        gj_i = gk[1][None, :, :]
        pk = pauli_k[:, None, :]
        src_k = jnp.stack([pk * (gi_r * gj_r - gi_i * gj_i), pk * (gi_r * gj_i + gi_i * gj_r)])
        lad_kb = lad_k[:, None, :]

        def left_mul(x):
            shp = x.shape
            flat = x.reshape(2 * shp[1], shp[2], shp[3])
            out = jnp.einsum("ab,bmn->amn", h_big, flat, precision=highest)
            return out.reshape(shp)

        def right_mul(x):
            xr = x[0]
            xi = x[1]
            out_re = jnp.einsum("ikj,nj->ikn", xr, hre, precision=highest) - jnp.einsum(
                "ikj,nj->ikn", xi, him, precision=highest
            )
            out_im = jnp.einsum("ikj,nj->ikn", xr, him, precision=highest) + jnp.einsum(
                "ikj,nj->ikn", xi, hre, precision=highest
            )
            return jnp.stack([out_re, out_im])

        def apply_ij(x):
            return left_mul(x) + right_mul(x)

        def to_k(x):
            xs = x.reshape(2, ndev, kb, nrows, ncols)
            got = lax.all_to_all(xs, ("row", "col"), 1, 1, tiled=True)
            got = got.reshape(2, nrow, ncol, kb, nrows, ncols).transpose(0, 1, 4, 3, 2, 5)
            return got.reshape(2, nrow * nrows, kb, ncol * ncols)

        def from_k(y):
            ys = y.reshape(2, nrow, nrows, kb, ncol, ncols).transpose(0, 1, 4, 3, 2, 5)
            ys = ys.reshape(2, ndev, kb, nrows, ncols)
            got = lax.all_to_all(ys, ("row", "col"), 1, 1, tiled=True)
            return got.reshape(2, orbs, nrows, ncols)

        dt = time_step
        dt2 = 0.5 * time_step * time_step
        g = green
        g_k = to_k(g)
        p = left_mul(g)
        p_k = to_k(p)
        q = apply_ij(g_k) + lad_kb * g_k
        e = p_k + q + src_k
        w = e + p_k
        part_k = neg_i(q, dt) - dt2 * (apply_ij(w) + lad_kb * e)
        part_k_a = from_k(part_k)
        e2 = p + lad_a * g + src_a
        part_a = g + neg_i(p + src_a, dt) - dt2 * left_mul(e2)
        return part_a + part_k_a

    return on_device


def solution(mesh):
    placed = (
        P("grp", None, "row", "col"),
        P("grp", None, None),
        P("grp", None, None),
        P(),
        P(),
        P(),
        P(),
    )
    return jax.shard_map(
        make_on_device(mesh.shape["row"], mesh.shape["col"]),
        mesh=mesh,
        in_specs=placed,
        out_specs=P("grp", None, "row", "col"),
        check_vma=False,
    )
```

```python
import jax
import jax.numpy as jnp
from jax import lax
from jax.sharding import PartitionSpec as P

time_step = 0.1
highest = lax.Precision.HIGHEST


def neg_i(x, scale):
    return jnp.stack([scale * x[1], -scale * x[0]])


def make_on_device(nrow, ncol):
    ndev = nrow * ncol

    def on_device(green, hamiltonian, onebody, site_map, onsite_u, pair_first, pair_second):
        orbs = green.shape[1]
        nrows = green.shape[2]
        ncols = green.shape[3]
        kb = orbs // ndev
        r = lax.axis_index("row")
        c = lax.axis_index("col")
        row_start = r * nrows
        col_start = c * ncols
        k_start = (r * ncol + c) * kb
        levels = jnp.arange(onsite_u.shape[0], dtype=jnp.int32)
        orb_ids = jnp.arange(orbs, dtype=jnp.int32)
        u_all = jnp.sum(jnp.where(site_map[:, None] == levels[None, :], onsite_u[None, :], 0.0), axis=1)
        first_hot = (pair_first[:, None] == orb_ids[None, :]).astype(jnp.float32)
        second_hot = (pair_second[:, None] == orb_ids[None, :]).astype(jnp.float32)
        hre = hamiltonian[0]
        him = hamiltonian[1]
        h_big = jnp.concatenate(
            [jnp.concatenate([hre, -him], axis=1), jnp.concatenate([him, hre], axis=1)], axis=0
        )

        sites_i = lax.dynamic_slice_in_dim(site_map, row_start, nrows)
        sites_j = lax.dynamic_slice_in_dim(site_map, col_start, ncols)
        u_i = lax.dynamic_slice_in_dim(u_all, row_start, nrows)
        lad_a = u_i[:, None] * (sites_i[:, None] == sites_j[None, :]).astype(jnp.float32)
        fh_a = lax.dynamic_slice_in_dim(first_hot, row_start, nrows, 1)
        sh_a = lax.dynamic_slice_in_dim(second_hot, col_start, ncols, 1)
        pauli_a = u_i[:, None] * jnp.einsum("pi,pj->ij", fh_a, sh_a, precision=highest)
        left = lax.dynamic_slice_in_dim(onebody, row_start, nrows, 2)
        right = lax.dynamic_slice_in_dim(onebody, col_start, ncols, 2)
        src_a = jnp.stack([
            pauli_a * (left[0][:, :, None] * right[0][:, None, :] - left[1][:, :, None] * right[1][:, None, :]),
            pauli_a * (left[0][:, :, None] * right[1][:, None, :] + left[1][:, :, None] * right[0][:, None, :]),
        ])

        lad_k = u_all[:, None] * (site_map[:, None] == site_map[None, :]).astype(jnp.float32)
        pauli_k = u_all[:, None] * jnp.einsum("pi,pj->ij", first_hot, second_hot, precision=highest)
        gk = lax.dynamic_slice_in_dim(onebody, k_start, kb, 1)
        gi_r = gk[0][:, :, None]
        gi_i = gk[1][:, :, None]
        gj_r = gk[0][:, None, :]
        gj_i = gk[1][:, None, :]
        pk = pauli_k[None, :, :]
        src_k = jnp.stack([pk * (gi_r * gj_r - gi_i * gj_i), pk * (gi_r * gj_i + gi_i * gj_r)])
        lad_kb = lad_k[None, :, :]

        def left_mul(x):
            shp = x.shape
            flat = x.reshape(2 * shp[1], shp[2], shp[3])
            out = jnp.einsum("ab,bmn->amn", h_big, flat, precision=highest)
            return out.reshape(shp)

        def apply_ij(x):
            xr = x[0]
            xi = x[1]

            def li(hm, xm):
                return jnp.einsum("ia,kaj->kij", hm, xm, precision=highest)

            def lj(xm, hm):
                return jnp.einsum("kia,ja->kij", xm, hm, precision=highest)

            out_re = li(hre, xr) - li(him, xi) + lj(xr, hre) - lj(xi, him)
            out_im = li(hre, xi) + li(him, xr) + lj(xi, hre) + lj(xr, him)
            return jnp.stack([out_re, out_im])

        def to_k(x):
            xs = x.reshape(2, ndev, kb, nrows, ncols)
            got = lax.all_to_all(xs, ("row", "col"), 1, 1, tiled=True)
            rows = [
                jnp.concatenate([got[:, a * ncol + b] for b in range(ncol)], axis=-1)
                for a in range(nrow)
            ]
            return jnp.concatenate(rows, axis=-2)

        def from_k(y):
            ys = jnp.stack(
                [
                    y[:, :, a * nrows:(a + 1) * nrows, b * ncols:(b + 1) * ncols]
                    for a in range(nrow)
                    for b in range(ncol)
                ],
                axis=1,
            )
            got = lax.all_to_all(ys, ("row", "col"), 1, 1, tiled=True)
            return got.reshape(2, orbs, nrows, ncols)

        dt = time_step
        dt2 = 0.5 * time_step * time_step
        g = green
        g_k = to_k(g)
        p = left_mul(g)
        p_k = to_k(p)
        q = apply_ij(g_k) + lad_kb * g_k
        e = p_k + q + src_k
        w = e + p_k
        part_k = neg_i(q, dt) - dt2 * (apply_ij(w) + lad_kb * e)
        part_k_a = from_k(part_k)
        e2 = p + lad_a * g + src_a
        part_a = g + neg_i(p + src_a, dt) - dt2 * left_mul(e2)
        return part_a + part_k_a

    return on_device


def solution(mesh):
    placed = (
        P("grp", None, "row", "col"),
        P("grp", None, None),
        P("grp", None, None),
        P(),
        P(),
        P(),
        P(),
    )
    return jax.shard_map(
        make_on_device(mesh.shape["row"], mesh.shape["col"]),
        mesh=mesh,
        in_specs=placed,
        out_specs=P("grp", None, "row", "col"),
        check_vma=False,
    )
```

```python
import jax
import jax.numpy as jnp
from jax import lax
from jax.sharding import PartitionSpec as P

time_step = 0.1
matmul_precision = lax.Precision.HIGH


def neg_i(x, scale):
    return jnp.stack([scale * x[1], -scale * x[0]])


def make_on_device(nrow, ncol):
    ndev = nrow * ncol

    def on_device(green, hamiltonian, onebody, site_map, onsite_u, pair_first, pair_second):
        orbs = green.shape[1]
        nrows = green.shape[2]
        ncols = green.shape[3]
        kb = orbs // ndev
        r = lax.axis_index("row")
        c = lax.axis_index("col")
        row_start = r * nrows
        col_start = c * ncols
        k_start = (r * ncol + c) * kb
        levels = jnp.arange(onsite_u.shape[0], dtype=jnp.int32)
        orb_ids = jnp.arange(orbs, dtype=jnp.int32)
        u_all = jnp.sum(jnp.where(site_map[:, None] == levels[None, :], onsite_u[None, :], 0.0), axis=1)
        first_hot = (pair_first[:, None] == orb_ids[None, :]).astype(jnp.float32)
        second_hot = (pair_second[:, None] == orb_ids[None, :]).astype(jnp.float32)
        hre = hamiltonian[0]
        him = hamiltonian[1]
        h_big = jnp.concatenate(
            [jnp.concatenate([hre, -him], axis=1), jnp.concatenate([him, hre], axis=1)], axis=0
        )

        sites_i = lax.dynamic_slice_in_dim(site_map, row_start, nrows)
        sites_j = lax.dynamic_slice_in_dim(site_map, col_start, ncols)
        u_i = lax.dynamic_slice_in_dim(u_all, row_start, nrows)
        lad_a = u_i[:, None] * (sites_i[:, None] == sites_j[None, :]).astype(jnp.float32)
        fh_a = lax.dynamic_slice_in_dim(first_hot, row_start, nrows, 1)
        sh_a = lax.dynamic_slice_in_dim(second_hot, col_start, ncols, 1)
        pauli_a = u_i[:, None] * jnp.einsum("pi,pj->ij", fh_a, sh_a, precision=matmul_precision)
        left = lax.dynamic_slice_in_dim(onebody, row_start, nrows, 2)
        right = lax.dynamic_slice_in_dim(onebody, col_start, ncols, 2)
        src_a = jnp.stack([
            pauli_a * (left[0][:, :, None] * right[0][:, None, :] - left[1][:, :, None] * right[1][:, None, :]),
            pauli_a * (left[0][:, :, None] * right[1][:, None, :] + left[1][:, :, None] * right[0][:, None, :]),
        ])

        lad_k = u_all[:, None] * (site_map[:, None] == site_map[None, :]).astype(jnp.float32)
        pauli_k = u_all[:, None] * jnp.einsum("pi,pj->ij", first_hot, second_hot, precision=matmul_precision)
        gk = lax.dynamic_slice_in_dim(onebody, k_start, kb, 1)
        gi_r = gk[0][:, :, None]
        gi_i = gk[1][:, :, None]
        gj_r = gk[0][:, None, :]
        gj_i = gk[1][:, None, :]
        pk = pauli_k[None, :, :]
        src_k = jnp.stack([pk * (gi_r * gj_r - gi_i * gj_i), pk * (gi_r * gj_i + gi_i * gj_r)])
        lad_kb = lad_k[None, :, :]

        def left_mul(x):
            shp = x.shape
            flat = x.reshape(2 * shp[1], shp[2], shp[3])
            out = jnp.einsum("ab,bmn->amn", h_big, flat, precision=matmul_precision)
            return out.reshape(shp)

        def apply_ij(x):
            xr = x[0]
            xi = x[1]

            def li(hm, xm):
                return jnp.einsum("ia,kaj->kij", hm, xm, precision=matmul_precision)

            def lj(xm, hm):
                return jnp.einsum("kia,ja->kij", xm, hm, precision=matmul_precision)

            out_re = li(hre, xr) - li(him, xi) + lj(xr, hre) - lj(xi, him)
            out_im = li(hre, xi) + li(him, xr) + lj(xi, hre) + lj(xr, him)
            return jnp.stack([out_re, out_im])

        def to_k(x):
            xs = x.reshape(2, ndev, kb, nrows, ncols)
            got = lax.all_to_all(xs, ("row", "col"), 1, 1, tiled=True)
            rows = [
                jnp.concatenate([got[:, a * ncol + b] for b in range(ncol)], axis=-1)
                for a in range(nrow)
            ]
            return jnp.concatenate(rows, axis=-2)

        def from_k(y):
            ys = jnp.stack(
                [
                    y[:, :, a * nrows:(a + 1) * nrows, b * ncols:(b + 1) * ncols]
                    for a in range(nrow)
                    for b in range(ncol)
                ],
                axis=1,
            )
            got = lax.all_to_all(ys, ("row", "col"), 1, 1, tiled=True)
            return got.reshape(2, orbs, nrows, ncols)

        dt = time_step
        dt2 = 0.5 * time_step * time_step
        g = green
        g_k = to_k(g)
        p = left_mul(g)
        p_k = to_k(p)
        q = apply_ij(g_k) + lad_kb * g_k
        e = p_k + q + src_k
        w = e + p_k
        part_k = neg_i(q, dt) - dt2 * (apply_ij(w) + lad_kb * e)
        part_k_a = from_k(part_k)
        e2 = p + lad_a * g + src_a
        part_a = g + neg_i(p + src_a, dt) - dt2 * left_mul(e2)
        return part_a + part_k_a

    return on_device


def solution(mesh):
    placed = (
        P("grp", None, "row", "col"),
        P("grp", None, None),
        P("grp", None, None),
        P(),
        P(),
        P(),
        P(),
    )
    return jax.shard_map(
        make_on_device(mesh.shape["row"], mesh.shape["col"]),
        mesh=mesh,
        in_specs=placed,
        out_specs=P("grp", None, "row", "col"),
        check_vma=False,
    )
```

```python
import jax
import jax.numpy as jnp
from jax import lax
from jax.sharding import PartitionSpec as P

time_step = 0.1
matmul_precision = lax.Precision.HIGH


def neg_i(x, scale):
    return jnp.stack([scale * x[1], -scale * x[0]])


def make_on_device(nrow, ncol):
    ndev = nrow * ncol

    def on_device(green, hamiltonian, onebody, site_map, onsite_u, pair_first, pair_second):
        orbs = green.shape[1]
        nrows = green.shape[2]
        ncols = green.shape[3]
        kb = orbs // ndev
        r = lax.axis_index("row")
        c = lax.axis_index("col")
        row_start = r * nrows
        col_start = c * ncols
        k_start = (r * ncol + c) * kb
        levels = jnp.arange(onsite_u.shape[0], dtype=jnp.int32)
        orb_ids = jnp.arange(orbs, dtype=jnp.int32)
        u_all = jnp.sum(jnp.where(site_map[:, None] == levels[None, :], onsite_u[None, :], 0.0), axis=1)
        first_hot = (pair_first[:, None] == orb_ids[None, :]).astype(jnp.float32)
        second_hot = (pair_second[:, None] == orb_ids[None, :]).astype(jnp.float32)
        hre = hamiltonian[0]
        him = hamiltonian[1]
        h_big = jnp.concatenate(
            [jnp.concatenate([hre, -him], axis=1), jnp.concatenate([him, hre], axis=1)], axis=0
        )

        sites_i = lax.dynamic_slice_in_dim(site_map, row_start, nrows)
        sites_j = lax.dynamic_slice_in_dim(site_map, col_start, ncols)
        u_i = lax.dynamic_slice_in_dim(u_all, row_start, nrows)
        lad_a = u_i[:, None] * (sites_i[:, None] == sites_j[None, :]).astype(jnp.float32)
        fh_a = lax.dynamic_slice_in_dim(first_hot, row_start, nrows, 1)
        sh_a = lax.dynamic_slice_in_dim(second_hot, col_start, ncols, 1)
        pauli_a = u_i[:, None] * jnp.einsum("pi,pj->ij", fh_a, sh_a, precision=matmul_precision)
        left = lax.dynamic_slice_in_dim(onebody, row_start, nrows, 2)
        right = lax.dynamic_slice_in_dim(onebody, col_start, ncols, 2)
        src_a = jnp.stack([
            pauli_a * (left[0][:, :, None] * right[0][:, None, :] - left[1][:, :, None] * right[1][:, None, :]),
            pauli_a * (left[0][:, :, None] * right[1][:, None, :] + left[1][:, :, None] * right[0][:, None, :]),
        ])

        lad_k = u_all[:, None] * (site_map[:, None] == site_map[None, :]).astype(jnp.float32)
        pauli_k = u_all[:, None] * jnp.einsum("pi,pj->ij", first_hot, second_hot, precision=matmul_precision)
        gk = lax.dynamic_slice_in_dim(onebody, k_start, kb, 1)
        gi_r = gk[0][:, :, None]
        gi_i = gk[1][:, :, None]
        gj_r = gk[0][:, None, :]
        gj_i = gk[1][:, None, :]
        pk = pauli_k[None, :, :]
        src_k = jnp.stack([pk * (gi_r * gj_r - gi_i * gj_i), pk * (gi_r * gj_i + gi_i * gj_r)])
        lad_kb = lad_k[None, :, :]

        def left_mul(x):
            shp = x.shape
            flat = x.reshape(2 * shp[1], shp[2], shp[3])
            out = jnp.einsum("ab,bmn->amn", h_big, flat, precision=matmul_precision)
            return out.reshape(shp)

        def apply_ij(x):
            xr = x[0]
            xi = x[1]

            def li(hm, xm):
                return jnp.einsum("ia,kaj->kij", hm, xm, precision=matmul_precision)

            def lj(xm, hm):
                return jnp.einsum("kia,ja->kij", xm, hm, precision=matmul_precision)

            out_re = li(hre, xr) - li(him, xi) + lj(xr, hre) - lj(xi, him)
            out_im = li(hre, xi) + li(him, xr) + lj(xi, hre) + lj(xr, him)
            return jnp.stack([out_re, out_im])

        def to_k(x):
            lead = x.shape[0]
            xs = x.reshape(lead, ndev, kb, nrows, ncols)
            got = lax.all_to_all(xs, ("row", "col"), 1, 1, tiled=True)
            rows = [
                jnp.concatenate([got[:, a * ncol + b] for b in range(ncol)], axis=-1)
                for a in range(nrow)
            ]
            return jnp.concatenate(rows, axis=-2)

        def from_k(y):
            ys = jnp.stack(
                [
                    y[:, :, a * nrows:(a + 1) * nrows, b * ncols:(b + 1) * ncols]
                    for a in range(nrow)
                    for b in range(ncol)
                ],
                axis=1,
            )
            return lax.all_to_all(ys, ("row", "col"), 1, 1, tiled=True)

        dt = time_step
        dt2 = 0.5 * time_step * time_step
        g = green
        p = left_mul(g)
        gp_k = to_k(jnp.concatenate([g, p]))
        e2 = p + lad_a * g + src_a
        part_a = g + neg_i(p + src_a, dt) - dt2 * left_mul(e2)
        gp_k, part_a = lax.optimization_barrier((gp_k, part_a))
        nchunk = 2
        kc = kb // nchunk
        backs = []
        for h in range(nchunk):
            sl = slice(h * kc, (h + 1) * kc)
            g_k = gp_k[:2, sl]
            p_k = gp_k[2:, sl]
            src_h = src_k[:, sl]
            q = apply_ij(g_k) + lad_kb * g_k
            e = p_k + q + src_h
            w = e + p_k
            part_k = neg_i(q, dt) - dt2 * (apply_ij(w) + lad_kb * e)
            backs.append(from_k(part_k))
        back = jnp.stack(backs, axis=2).reshape(2, orbs, nrows, ncols)
        return part_a + back

    return on_device


def solution(mesh):
    placed = (
        P("grp", None, "row", "col"),
        P("grp", None, None),
        P("grp", None, None),
        P(),
        P(),
        P(),
        P(),
    )
    return jax.shard_map(
        make_on_device(mesh.shape["row"], mesh.shape["col"]),
        mesh=mesh,
        in_specs=placed,
        out_specs=P("grp", None, "row", "col"),
        check_vma=False,
    )
```

```python
import jax
import jax.numpy as jnp
from jax import lax
from jax.sharding import PartitionSpec as P

time_step = 0.1
matmul_precision = lax.Precision.HIGH


def neg_i(x, scale):
    return jnp.stack([scale * x[1], -scale * x[0]])


def make_on_device(nrow, ncol):
    ndev = nrow * ncol

    def on_device(green, hamiltonian, onebody, site_map, onsite_u, pair_first, pair_second):
        orbs = green.shape[1]
        nrows = green.shape[2]
        ncols = green.shape[3]
        kb = orbs // ndev
        r = lax.axis_index("row")
        c = lax.axis_index("col")
        row_start = r * nrows
        col_start = c * ncols
        k_start = (r * ncol + c) * kb
        levels = jnp.arange(onsite_u.shape[0], dtype=jnp.int32)
        orb_ids = jnp.arange(orbs, dtype=jnp.int32)
        u_all = jnp.sum(jnp.where(site_map[:, None] == levels[None, :], onsite_u[None, :], 0.0), axis=1)
        first_hot = (pair_first[:, None] == orb_ids[None, :]).astype(jnp.float32)
        second_hot = (pair_second[:, None] == orb_ids[None, :]).astype(jnp.float32)
        hre = hamiltonian[0]
        him = hamiltonian[1]
        h_big = jnp.concatenate(
            [jnp.concatenate([hre, -him], axis=1), jnp.concatenate([him, hre], axis=1)], axis=0
        )

        sites_i = lax.dynamic_slice_in_dim(site_map, row_start, nrows)
        sites_j = lax.dynamic_slice_in_dim(site_map, col_start, ncols)
        u_i = lax.dynamic_slice_in_dim(u_all, row_start, nrows)
        lad_a = u_i[:, None] * (sites_i[:, None] == sites_j[None, :]).astype(jnp.float32)
        fh_a = lax.dynamic_slice_in_dim(first_hot, row_start, nrows, 1)
        sh_a = lax.dynamic_slice_in_dim(second_hot, col_start, ncols, 1)
        pauli_a = u_i[:, None] * jnp.einsum("pi,pj->ij", fh_a, sh_a, precision=matmul_precision)
        left = lax.dynamic_slice_in_dim(onebody, row_start, nrows, 2)
        right = lax.dynamic_slice_in_dim(onebody, col_start, ncols, 2)
        src_a = jnp.stack([
            pauli_a * (left[0][:, :, None] * right[0][:, None, :] - left[1][:, :, None] * right[1][:, None, :]),
            pauli_a * (left[0][:, :, None] * right[1][:, None, :] + left[1][:, :, None] * right[0][:, None, :]),
        ])

        lad_k = u_all[:, None] * (site_map[:, None] == site_map[None, :]).astype(jnp.float32)
        pauli_k = u_all[:, None] * jnp.einsum("pi,pj->ij", first_hot, second_hot, precision=matmul_precision)
        gk = lax.dynamic_slice_in_dim(onebody, k_start, kb, 1)
        gi_r = gk[0][:, :, None]
        gi_i = gk[1][:, :, None]
        gj_r = gk[0][:, None, :]
        gj_i = gk[1][:, None, :]
        pk = pauli_k[None, :, :]
        src_k = jnp.stack([pk * (gi_r * gj_r - gi_i * gj_i), pk * (gi_r * gj_i + gi_i * gj_r)])
        lad_kb = lad_k[None, :, :]

        def left_mul(x):
            shp = x.shape
            flat = x.reshape(2 * shp[1], shp[2], shp[3])
            out = jnp.einsum("ab,bmn->amn", h_big, flat, precision=matmul_precision)
            return out.reshape(shp)

        def apply_ij(x):
            xr = x[0]
            xi = x[1]

            def li(hm, xm):
                return jnp.einsum("ia,kaj->kij", hm, xm, precision=matmul_precision)

            def lj(xm, hm):
                return jnp.einsum("kia,ja->kij", xm, hm, precision=matmul_precision)

            out_re = li(hre, xr) - li(him, xi) + lj(xr, hre) - lj(xi, him)
            out_im = li(hre, xi) + li(him, xr) + lj(xi, hre) + lj(xr, him)
            return jnp.stack([out_re, out_im])

        def to_k(x):
            lead = x.shape[0]
            xs = x.reshape(lead, ndev, kb, nrows, ncols)
            got = lax.all_to_all(xs, ("row", "col"), 1, 1, tiled=True)
            rows = [
                jnp.concatenate([got[:, a * ncol + b] for b in range(ncol)], axis=-1)
                for a in range(nrow)
            ]
            return jnp.concatenate(rows, axis=-2)

        def from_k(y):
            ys = jnp.stack(
                [
                    y[:, :, a * nrows:(a + 1) * nrows, b * ncols:(b + 1) * ncols]
                    for a in range(nrow)
                    for b in range(ncol)
                ],
                axis=1,
            )
            return lax.all_to_all(ys, ("row", "col"), 1, 1, tiled=True)

        dt = time_step
        dt2 = 0.5 * time_step * time_step
        g = green
        p = left_mul(g)
        gp_k = to_k(jnp.concatenate([g, p]))
        e2 = p + lad_a * g + src_a
        part_a = g + neg_i(p + src_a, dt) - dt2 * left_mul(e2)
        gp_k, part_a = lax.optimization_barrier((gp_k, part_a))
        nchunk = 1
        kc = kb // nchunk
        backs = []
        for h in range(nchunk):
            sl = slice(h * kc, (h + 1) * kc)
            g_k = gp_k[:2, sl]
            p_k = gp_k[2:, sl]
            src_h = src_k[:, sl]
            q = apply_ij(g_k) + lad_kb * g_k
            e = p_k + q + src_h
            w = e + p_k
            part_k = neg_i(q, dt) - dt2 * (apply_ij(w) + lad_kb * e)
            backs.append(from_k(part_k))
        back = jnp.stack(backs, axis=2).reshape(2, orbs, nrows, ncols)
        return part_a + back

    return on_device


def solution(mesh):
    placed = (
        P("grp", None, "row", "col"),
        P("grp", None, None),
        P("grp", None, None),
        P(),
        P(),
        P(),
        P(),
    )
    return jax.shard_map(
        make_on_device(mesh.shape["row"], mesh.shape["col"]),
        mesh=mesh,
        in_specs=placed,
        out_specs=P("grp", None, "row", "col"),
        check_vma=False,
    )
```

```python
import jax
import jax.numpy as jnp
from jax import lax
from jax.sharding import PartitionSpec as P

time_step = 0.1
matmul_precision = lax.Precision.HIGH


def neg_i(x, scale):
    return jnp.stack([scale * x[1], -scale * x[0]])


def make_on_device(nrow, ncol):
    ndev = nrow * ncol

    def on_device(green, hamiltonian, onebody, site_map, onsite_u, pair_first, pair_second):
        orbs = green.shape[1]
        nrows = green.shape[2]
        ncols = green.shape[3]
        kb = orbs // ndev
        r = lax.axis_index("row")
        c = lax.axis_index("col")
        row_start = r * nrows
        col_start = c * ncols
        k_start = (r * ncol + c) * kb
        levels = jnp.arange(onsite_u.shape[0], dtype=jnp.int32)
        orb_ids = jnp.arange(orbs, dtype=jnp.int32)
        u_all = jnp.sum(jnp.where(site_map[:, None] == levels[None, :], onsite_u[None, :], 0.0), axis=1)
        first_hot = (pair_first[:, None] == orb_ids[None, :]).astype(jnp.float32)
        second_hot = (pair_second[:, None] == orb_ids[None, :]).astype(jnp.float32)
        hre = hamiltonian[0]
        him = hamiltonian[1]
        h_big = jnp.concatenate(
            [jnp.concatenate([hre, -him], axis=1), jnp.concatenate([him, hre], axis=1)], axis=0
        )

        sites_i = lax.dynamic_slice_in_dim(site_map, row_start, nrows)
        sites_j = lax.dynamic_slice_in_dim(site_map, col_start, ncols)
        u_i = lax.dynamic_slice_in_dim(u_all, row_start, nrows)
        lad_a = u_i[:, None] * (sites_i[:, None] == sites_j[None, :]).astype(jnp.float32)
        fh_a = lax.dynamic_slice_in_dim(first_hot, row_start, nrows, 1)
        sh_a = lax.dynamic_slice_in_dim(second_hot, col_start, ncols, 1)
        pauli_a = u_i[:, None] * jnp.einsum("pi,pj->ij", fh_a, sh_a, precision=matmul_precision)
        left = lax.dynamic_slice_in_dim(onebody, row_start, nrows, 2)
        right = lax.dynamic_slice_in_dim(onebody, col_start, ncols, 2)
        src_a = jnp.stack([
            pauli_a * (left[0][:, :, None] * right[0][:, None, :] - left[1][:, :, None] * right[1][:, None, :]),
            pauli_a * (left[0][:, :, None] * right[1][:, None, :] + left[1][:, :, None] * right[0][:, None, :]),
        ])

        lad_k = u_all[:, None] * (site_map[:, None] == site_map[None, :]).astype(jnp.float32)
        pauli_k = u_all[:, None] * jnp.einsum("pi,pj->ij", first_hot, second_hot, precision=matmul_precision)
        gk = lax.dynamic_slice_in_dim(onebody, k_start, kb, 1)
        gi_r = gk[0][:, :, None]
        gi_i = gk[1][:, :, None]
        gj_r = gk[0][:, None, :]
        gj_i = gk[1][:, None, :]
        pk = pauli_k[None, :, :]
        src_k = jnp.stack([pk * (gi_r * gj_r - gi_i * gj_i), pk * (gi_r * gj_i + gi_i * gj_r)])
        lad_kb = lad_k[None, :, :]

        def left_mul(x):
            shp = x.shape
            flat = x.reshape(2 * shp[1], shp[2], shp[3])
            out = jnp.einsum("ab,bmn->amn", h_big, flat, precision=matmul_precision)
            return out.reshape(shp)

        def apply_ij(x):
            xr = x[0]
            xi = x[1]

            def li(hm, xm):
                return jnp.einsum("ia,kaj->kij", hm, xm, precision=matmul_precision)

            def lj(xm, hm):
                return jnp.einsum("kia,ja->kij", xm, hm, precision=matmul_precision)

            out_re = li(hre, xr) - li(him, xi) + lj(xr, hre) - lj(xi, him)
            out_im = li(hre, xi) + li(him, xr) + lj(xi, hre) + lj(xr, him)
            return jnp.stack([out_re, out_im])

        def to_k(x):
            xs = x.reshape(2, ndev, kb, nrows, ncols)
            got = lax.all_to_all(xs, ("row", "col"), 1, 1, tiled=True)
            rows = [
                jnp.concatenate([got[:, a * ncol + b] for b in range(ncol)], axis=-1)
                for a in range(nrow)
            ]
            return jnp.concatenate(rows, axis=-2)

        def send_k(y):
            return jnp.stack(
                [
                    y[:, :, a * nrows:(a + 1) * nrows, b * ncols:(b + 1) * ncols]
                    for a in range(nrow)
                    for b in range(ncol)
                ],
                axis=1,
            )

        def recv_k(ys):
            got = lax.all_to_all(ys, ("row", "col"), 1, 1, tiled=True)
            return got.reshape(2, orbs, nrows, ncols)

        dt = time_step
        dt2 = 0.5 * time_step * time_step
        g = green
        g_k = to_k(g)
        p = left_mul(g)
        p_k = to_k(p)
        q = apply_ij(g_k) + lad_kb * g_k
        e = p_k + q + src_k
        w = e + p_k
        part_k = neg_i(q, dt) - dt2 * (apply_ij(w) + lad_kb * e)
        ys, g2, p2 = lax.optimization_barrier((send_k(part_k), g, p))
        part_k_a = recv_k(ys)
        e2 = p2 + lad_a * g2 + src_a
        part_a = g2 + neg_i(p2 + src_a, dt) - dt2 * left_mul(e2)
        part_a = lax.optimization_barrier(part_a)
        return part_a + part_k_a

    return on_device


def solution(mesh):
    placed = (
        P("grp", None, "row", "col"),
        P("grp", None, None),
        P("grp", None, None),
        P(),
        P(),
        P(),
        P(),
    )
    return jax.shard_map(
        make_on_device(mesh.shape["row"], mesh.shape["col"]),
        mesh=mesh,
        in_specs=placed,
        out_specs=P("grp", None, "row", "col"),
        check_vma=False,
    )
```

```python
import jax
import jax.numpy as jnp
from jax import lax
from jax.sharding import PartitionSpec as P

time_step = 0.1
matmul_precision = lax.Precision.HIGH


def neg_i(x, scale):
    return jnp.stack([scale * x[1], -scale * x[0]])


def make_on_device(nrow, ncol):
    ndev = nrow * ncol

    def on_device(green, hamiltonian, onebody, site_map, onsite_u, pair_first, pair_second):
        orbs = green.shape[1]
        nrows = green.shape[2]
        ncols = green.shape[3]
        kb = orbs // ndev
        r = lax.axis_index("row")
        c = lax.axis_index("col")
        row_start = r * nrows
        col_start = c * ncols
        k_start = (r * ncol + c) * kb
        levels = jnp.arange(onsite_u.shape[0], dtype=jnp.int32)
        orb_ids = jnp.arange(orbs, dtype=jnp.int32)
        u_all = jnp.sum(jnp.where(site_map[:, None] == levels[None, :], onsite_u[None, :], 0.0), axis=1)
        first_hot = (pair_first[:, None] == orb_ids[None, :]).astype(jnp.float32)
        second_hot = (pair_second[:, None] == orb_ids[None, :]).astype(jnp.float32)
        hre = hamiltonian[0]
        him = hamiltonian[1]
        h_big = jnp.concatenate(
            [jnp.concatenate([hre, -him], axis=1), jnp.concatenate([him, hre], axis=1)], axis=0
        )

        sites_i = lax.dynamic_slice_in_dim(site_map, row_start, nrows)
        sites_j = lax.dynamic_slice_in_dim(site_map, col_start, ncols)
        u_i = lax.dynamic_slice_in_dim(u_all, row_start, nrows)
        lad_a = u_i[:, None] * (sites_i[:, None] == sites_j[None, :]).astype(jnp.float32)
        fh_a = lax.dynamic_slice_in_dim(first_hot, row_start, nrows, 1)
        sh_a = lax.dynamic_slice_in_dim(second_hot, col_start, ncols, 1)
        pauli_a = u_i[:, None] * jnp.einsum("pi,pj->ij", fh_a, sh_a, precision=matmul_precision)
        left = lax.dynamic_slice_in_dim(onebody, row_start, nrows, 2)
        right = lax.dynamic_slice_in_dim(onebody, col_start, ncols, 2)
        src_a = jnp.stack([
            pauli_a * (left[0][:, :, None] * right[0][:, None, :] - left[1][:, :, None] * right[1][:, None, :]),
            pauli_a * (left[0][:, :, None] * right[1][:, None, :] + left[1][:, :, None] * right[0][:, None, :]),
        ])

        lad_k = u_all[:, None] * (site_map[:, None] == site_map[None, :]).astype(jnp.float32)
        pauli_k = u_all[:, None] * jnp.einsum("pi,pj->ij", first_hot, second_hot, precision=matmul_precision)
        gk = lax.dynamic_slice_in_dim(onebody, k_start, kb, 1)
        gi_r = gk[0][:, :, None]
        gi_i = gk[1][:, :, None]
        gj_r = gk[0][:, None, :]
        gj_i = gk[1][:, None, :]
        pk = pauli_k[None, :, :]
        src_k = jnp.stack([pk * (gi_r * gj_r - gi_i * gj_i), pk * (gi_r * gj_i + gi_i * gj_r)])
        lad_kb = lad_k[None, :, :]

        def left_mul(x):
            shp = x.shape
            flat = x.reshape(2 * shp[1], shp[2], shp[3])
            out = jnp.einsum("ab,bmn->amn", h_big, flat, precision=matmul_precision)
            return out.reshape(shp)

        def apply_ij(x):
            xr = x[0]
            xi = x[1]

            def li(hm, xm):
                return jnp.einsum("ia,kaj->kij", hm, xm, precision=matmul_precision)

            def lj(xm, hm):
                return jnp.einsum("kia,ja->kij", xm, hm, precision=matmul_precision)

            out_re = li(hre, xr) - li(him, xi) + lj(xr, hre) - lj(xi, him)
            out_im = li(hre, xi) + li(him, xr) + lj(xi, hre) + lj(xr, him)
            return jnp.stack([out_re, out_im])

        def to_k(x):
            xs = x.reshape(2, ndev, kb, nrows, ncols)
            got = lax.all_to_all(xs, ("row", "col"), 1, 1, tiled=True)
            rows = [
                jnp.concatenate([got[:, a * ncol + b] for b in range(ncol)], axis=-1)
                for a in range(nrow)
            ]
            return jnp.concatenate(rows, axis=-2)

        def send_k(y):
            return jnp.stack(
                [
                    y[:, :, a * nrows:(a + 1) * nrows, b * ncols:(b + 1) * ncols]
                    for a in range(nrow)
                    for b in range(ncol)
                ],
                axis=1,
            )

        def recv_k(ys):
            got = lax.all_to_all(ys, ("row", "col"), 1, 1, tiled=True)
            return got.reshape(2, orbs, nrows, ncols)

        dt = time_step
        dt2 = 0.5 * time_step * time_step
        g = green
        g_k = to_k(g)
        p = left_mul(g)
        p_k = to_k(p)
        q = apply_ij(g_k) + lad_kb * g_k
        pre = apply_ij(q + src_k)
        e = p_k + q + src_k
        part_k = neg_i(q, dt) - dt2 * (apply_ij(p_k + p_k) + pre + lad_kb * e)
        ys, g2, p2 = lax.optimization_barrier((send_k(part_k), g, p))
        part_k_a = recv_k(ys)
        e2 = p2 + lad_a * g2 + src_a
        part_a = g2 + neg_i(p2 + src_a, dt) - dt2 * left_mul(e2)
        part_a = lax.optimization_barrier(part_a)
        return part_a + part_k_a

    return on_device


def solution(mesh):
    placed = (
        P("grp", None, "row", "col"),
        P("grp", None, None),
        P("grp", None, None),
        P(),
        P(),
        P(),
        P(),
    )
    return jax.shard_map(
        make_on_device(mesh.shape["row"], mesh.shape["col"]),
        mesh=mesh,
        in_specs=placed,
        out_specs=P("grp", None, "row", "col"),
        check_vma=False,
    )
```

```python
import jax
import jax.numpy as jnp
from jax import lax
from jax.sharding import PartitionSpec as P
from jax.experimental.layout import Layout, with_layout_constraint

time_step = 0.1
matmul_precision = lax.Precision.HIGH


def neg_i(x, scale):
    return jnp.stack([scale * x[1], -scale * x[0]])


def make_on_device(nrow, ncol):
    ndev = nrow * ncol

    def on_device(green, hamiltonian, onebody, site_map, onsite_u, pair_first, pair_second):
        orbs = green.shape[1]
        nrows = green.shape[2]
        ncols = green.shape[3]
        kb = orbs // ndev
        r = lax.axis_index("row")
        c = lax.axis_index("col")
        row_start = r * nrows
        col_start = c * ncols
        k_start = (r * ncol + c) * kb
        levels = jnp.arange(onsite_u.shape[0], dtype=jnp.int32)
        orb_ids = jnp.arange(orbs, dtype=jnp.int32)
        u_all = jnp.sum(jnp.where(site_map[:, None] == levels[None, :], onsite_u[None, :], 0.0), axis=1)
        first_hot = (pair_first[:, None] == orb_ids[None, :]).astype(jnp.float32)
        second_hot = (pair_second[:, None] == orb_ids[None, :]).astype(jnp.float32)
        hre = hamiltonian[0]
        him = hamiltonian[1]
        h_big = jnp.concatenate(
            [jnp.concatenate([hre, -him], axis=1), jnp.concatenate([him, hre], axis=1)], axis=0
        )

        sites_i = lax.dynamic_slice_in_dim(site_map, row_start, nrows)
        sites_j = lax.dynamic_slice_in_dim(site_map, col_start, ncols)
        u_i = lax.dynamic_slice_in_dim(u_all, row_start, nrows)
        lad_a = u_i[:, None] * (sites_i[:, None] == sites_j[None, :]).astype(jnp.float32)
        fh_a = lax.dynamic_slice_in_dim(first_hot, row_start, nrows, 1)
        sh_a = lax.dynamic_slice_in_dim(second_hot, col_start, ncols, 1)
        pauli_a = u_i[:, None] * jnp.einsum("pi,pj->ij", fh_a, sh_a, precision=matmul_precision)
        left = lax.dynamic_slice_in_dim(onebody, row_start, nrows, 2)
        right = lax.dynamic_slice_in_dim(onebody, col_start, ncols, 2)
        src_a = jnp.stack([
            pauli_a * (left[0][:, :, None] * right[0][:, None, :] - left[1][:, :, None] * right[1][:, None, :]),
            pauli_a * (left[0][:, :, None] * right[1][:, None, :] + left[1][:, :, None] * right[0][:, None, :]),
        ])

        lad_k = u_all[:, None] * (site_map[:, None] == site_map[None, :]).astype(jnp.float32)
        pauli_k = u_all[:, None] * jnp.einsum("pi,pj->ij", first_hot, second_hot, precision=matmul_precision)
        gk = lax.dynamic_slice_in_dim(onebody, k_start, kb, 1)
        gi_r = gk[0][:, :, None]
        gi_i = gk[1][:, :, None]
        gj_r = gk[0][:, None, :]
        gj_i = gk[1][:, None, :]
        pk = pauli_k[None, :, :]
        src_k = jnp.stack([pk * (gi_r * gj_r - gi_i * gj_i), pk * (gi_r * gj_i + gi_i * gj_r)])
        lad_kb = lad_k[None, :, :]

        def left_mul(x):
            shp = x.shape
            flat = x.reshape(2 * shp[1], shp[2], shp[3])
            out = jnp.einsum("ab,bmn->amn", h_big, flat, precision=matmul_precision)
            return out.reshape(shp)

        def apply_ij(x):
            xr = x[0]
            xi = x[1]

            def li(hm, xm):
                return jnp.einsum("ia,kaj->kij", hm, xm, precision=matmul_precision)

            def lj(xm, hm):
                return jnp.einsum("kia,ja->kij", xm, hm, precision=matmul_precision)

            out_re = li(hre, xr) - li(him, xi) + lj(xr, hre) - lj(xi, him)
            out_im = li(hre, xi) + li(him, xr) + lj(xi, hre) + lj(xr, him)
            return jnp.stack([out_re, out_im])

        def to_k(x):
            xs = x.reshape(2, ndev, kb, nrows, ncols)
            got = lax.all_to_all(xs, ("row", "col"), 1, 1, tiled=True)
            rows = [
                jnp.concatenate([got[:, a * ncol + b] for b in range(ncol)], axis=-1)
                for a in range(nrow)
            ]
            return jnp.concatenate(rows, axis=-2)

        def send_k(y):
            return jnp.stack(
                [
                    y[:, :, a * nrows:(a + 1) * nrows, b * ncols:(b + 1) * ncols]
                    for a in range(nrow)
                    for b in range(ncol)
                ],
                axis=1,
            )

        def recv_k(ys):
            got = lax.all_to_all(ys, ("row", "col"), 1, 1, tiled=True)
            return got.reshape(2, orbs, nrows, ncols)

        dt = time_step
        dt2 = 0.5 * time_step * time_step
        g = green
        g_k = to_k(g)
        p = left_mul(g)
        p_k = to_k(p)
        q = apply_ij(g_k) + lad_kb * g_k
        e = p_k + q + src_k
        w = e + p_k
        part_k = neg_i(q, dt) - dt2 * (apply_ij(w) + lad_kb * e)
        ys, g2, p2 = lax.optimization_barrier((send_k(part_k), g, p))
        part_k_a = recv_k(ys)
        e2 = p2 + lad_a * g2 + src_a
        part_a = g2 + neg_i(p2 + src_a, dt) - dt2 * left_mul(e2)
        part_a = lax.optimization_barrier(with_layout_constraint(part_a, Layout((0, 1, 2, 3))))
        return part_a + part_k_a

    return on_device


def solution(mesh):
    placed = (
        P("grp", None, "row", "col"),
        P("grp", None, None),
        P("grp", None, None),
        P(),
        P(),
        P(),
        P(),
    )
    return jax.shard_map(
        make_on_device(mesh.shape["row"], mesh.shape["col"]),
        mesh=mesh,
        in_specs=placed,
        out_specs=P("grp", None, "row", "col"),
        check_vma=False,
    )
```

```python
import jax
import jax.numpy as jnp
from jax import lax
from jax.sharding import PartitionSpec as P
from jax.experimental.layout import Layout, with_layout_constraint

time_step = 0.1
matmul_precision = lax.Precision.HIGH


def neg_i(x, scale):
    return jnp.stack([scale * x[1], -scale * x[0]])


def make_on_device(nrow, ncol):
    ndev = nrow * ncol

    def on_device(green, hamiltonian, onebody, site_map, onsite_u, pair_first, pair_second):
        orbs = green.shape[1]
        nrows = green.shape[2]
        ncols = green.shape[3]
        kb = orbs // ndev
        r = lax.axis_index("row")
        c = lax.axis_index("col")
        row_start = r * nrows
        col_start = c * ncols
        k_start = (r * ncol + c) * kb
        levels = jnp.arange(onsite_u.shape[0], dtype=jnp.int32)
        orb_ids = jnp.arange(orbs, dtype=jnp.int32)
        u_all = jnp.sum(jnp.where(site_map[:, None] == levels[None, :], onsite_u[None, :], 0.0), axis=1)
        first_hot = (pair_first[:, None] == orb_ids[None, :]).astype(jnp.float32)
        second_hot = (pair_second[:, None] == orb_ids[None, :]).astype(jnp.float32)
        hre = hamiltonian[0]
        him = hamiltonian[1]
        h_big = jnp.concatenate(
            [jnp.concatenate([hre, -him], axis=1), jnp.concatenate([him, hre], axis=1)], axis=0
        )

        sites_i = lax.dynamic_slice_in_dim(site_map, row_start, nrows)
        sites_j = lax.dynamic_slice_in_dim(site_map, col_start, ncols)
        u_i = lax.dynamic_slice_in_dim(u_all, row_start, nrows)
        lad_a = u_i[:, None] * (sites_i[:, None] == sites_j[None, :]).astype(jnp.float32)
        fh_a = lax.dynamic_slice_in_dim(first_hot, row_start, nrows, 1)
        sh_a = lax.dynamic_slice_in_dim(second_hot, col_start, ncols, 1)
        pauli_a = u_i[:, None] * jnp.einsum("pi,pj->ij", fh_a, sh_a, precision=matmul_precision)
        left = lax.dynamic_slice_in_dim(onebody, row_start, nrows, 2)
        right = lax.dynamic_slice_in_dim(onebody, col_start, ncols, 2)
        src_a = jnp.stack([
            pauli_a * (left[0][:, :, None] * right[0][:, None, :] - left[1][:, :, None] * right[1][:, None, :]),
            pauli_a * (left[0][:, :, None] * right[1][:, None, :] + left[1][:, :, None] * right[0][:, None, :]),
        ])

        lad_k = u_all[:, None] * (site_map[:, None] == site_map[None, :]).astype(jnp.float32)
        pauli_k = u_all[:, None] * jnp.einsum("pi,pj->ij", first_hot, second_hot, precision=matmul_precision)
        gk = lax.dynamic_slice_in_dim(onebody, k_start, kb, 1)
        gi_r = gk[0][:, :, None]
        gi_i = gk[1][:, :, None]
        gj_r = gk[0][:, None, :]
        gj_i = gk[1][:, None, :]
        pk = pauli_k[None, :, :]
        src_k = jnp.stack([pk * (gi_r * gj_r - gi_i * gj_i), pk * (gi_r * gj_i + gi_i * gj_r)])
        lad_kb = lad_k[None, :, :]

        def left_mul(x):
            shp = x.shape
            flat = x.reshape(2 * shp[1], shp[2], shp[3])
            out = jnp.einsum("ab,bmn->amn", h_big, flat, precision=matmul_precision)
            return out.reshape(shp)

        def apply_ij(x):
            xr = x[0]
            xi = x[1]

            def li(hm, xm):
                return jnp.einsum("ia,kaj->kij", hm, xm, precision=matmul_precision)

            def lj(xm, hm):
                return jnp.einsum("kia,ja->kij", xm, hm, precision=matmul_precision)

            out_re = li(hre, xr) - li(him, xi) + lj(xr, hre) - lj(xi, him)
            out_im = li(hre, xi) + li(him, xr) + lj(xi, hre) + lj(xr, him)
            return jnp.stack([out_re, out_im])

        def to_k(x):
            xs = x.reshape(2, ndev, kb, nrows, ncols)
            got = lax.all_to_all(xs, ("row", "col"), 1, 1, tiled=True)
            rows = [
                jnp.concatenate([got[:, a * ncol + b] for b in range(ncol)], axis=-1)
                for a in range(nrow)
            ]
            return jnp.concatenate(rows, axis=-2)

        def send_k(y):
            return jnp.stack(
                [
                    y[:, :, a * nrows:(a + 1) * nrows, b * ncols:(b + 1) * ncols]
                    for a in range(nrow)
                    for b in range(ncol)
                ],
                axis=1,
            )

        def recv_k(ys):
            got = lax.all_to_all(ys, ("row", "col"), 1, 1, tiled=True)
            return got.reshape(2, orbs, nrows, ncols)

        dt = time_step
        dt2 = 0.5 * time_step * time_step
        g = green
        g_k = to_k(g)
        p = left_mul(g)
        p_k = to_k(p)
        q = apply_ij(g_k) + lad_kb * g_k
        e = p_k + q + src_k
        w = e + p_k
        aw = apply_ij(w)

        def blk(x, a, b):
            return x[..., a * nrows:(a + 1) * nrows, b * ncols:(b + 1) * ncols]

        blocks = [
            neg_i(blk(q, a, b), dt) - dt2 * (blk(aw, a, b) + blk(lad_kb, a, b) * blk(e, a, b))
            for a in range(nrow)
            for b in range(ncol)
        ]
        ys, g2, p2 = lax.optimization_barrier((jnp.stack(blocks, axis=1), g, p))
        part_k_a = recv_k(ys)
        e2 = p2 + lad_a * g2 + src_a
        part_a = g2 + neg_i(p2 + src_a, dt) - dt2 * left_mul(e2)
        part_a = lax.optimization_barrier(with_layout_constraint(part_a, Layout((0, 1, 2, 3))))
        return part_a + part_k_a

    return on_device


def solution(mesh):
    placed = (
        P("grp", None, "row", "col"),
        P("grp", None, None),
        P("grp", None, None),
        P(),
        P(),
        P(),
        P(),
    )
    return jax.shard_map(
        make_on_device(mesh.shape["row"], mesh.shape["col"]),
        mesh=mesh,
        in_specs=placed,
        out_specs=P("grp", None, "row", "col"),
        check_vma=False,
    )
```

```python
import jax
import jax.numpy as jnp
from jax import lax
from jax.sharding import PartitionSpec as P
from jax.experimental.layout import Layout, with_layout_constraint

time_step = 0.1
matmul_precision = lax.Precision.HIGH


def neg_i(x, scale):
    return jnp.stack([scale * x[1], -scale * x[0]])


def make_on_device(nrow, ncol):
    ndev = nrow * ncol

    def on_device(green, hamiltonian, onebody, site_map, onsite_u, pair_first, pair_second):
        orbs = green.shape[1]
        nrows = green.shape[2]
        ncols = green.shape[3]
        kb = orbs // ndev
        r = lax.axis_index("row")
        c = lax.axis_index("col")
        row_start = r * nrows
        col_start = c * ncols
        k_start = (r * ncol + c) * kb
        levels = jnp.arange(onsite_u.shape[0], dtype=jnp.int32)
        orb_ids = jnp.arange(orbs, dtype=jnp.int32)
        u_all = jnp.sum(jnp.where(site_map[:, None] == levels[None, :], onsite_u[None, :], 0.0), axis=1)
        first_hot = (pair_first[:, None] == orb_ids[None, :]).astype(jnp.float32)
        second_hot = (pair_second[:, None] == orb_ids[None, :]).astype(jnp.float32)
        hre = hamiltonian[0]
        him = hamiltonian[1]
        h_big = jnp.concatenate(
            [jnp.concatenate([hre, -him], axis=1), jnp.concatenate([him, hre], axis=1)], axis=0
        )

        sites_i = lax.dynamic_slice_in_dim(site_map, row_start, nrows)
        sites_j = lax.dynamic_slice_in_dim(site_map, col_start, ncols)
        u_i = lax.dynamic_slice_in_dim(u_all, row_start, nrows)
        lad_a = u_i[:, None] * (sites_i[:, None] == sites_j[None, :]).astype(jnp.float32)
        fh_a = lax.dynamic_slice_in_dim(first_hot, row_start, nrows, 1)
        sh_a = lax.dynamic_slice_in_dim(second_hot, col_start, ncols, 1)
        pauli_a = u_i[:, None] * jnp.einsum("pi,pj->ij", fh_a, sh_a, precision=matmul_precision)
        left = lax.dynamic_slice_in_dim(onebody, row_start, nrows, 2)
        right = lax.dynamic_slice_in_dim(onebody, col_start, ncols, 2)
        src_a = jnp.stack([
            pauli_a * (left[0][:, :, None] * right[0][:, None, :] - left[1][:, :, None] * right[1][:, None, :]),
            pauli_a * (left[0][:, :, None] * right[1][:, None, :] + left[1][:, :, None] * right[0][:, None, :]),
        ])

        lad_k = u_all[:, None] * (site_map[:, None] == site_map[None, :]).astype(jnp.float32)
        pauli_k = u_all[:, None] * jnp.einsum("pi,pj->ij", first_hot, second_hot, precision=matmul_precision)
        gk = lax.dynamic_slice_in_dim(onebody, k_start, kb, 1)
        gi_r = gk[0][:, :, None]
        gi_i = gk[1][:, :, None]
        gj_r = gk[0][:, None, :]
        gj_i = gk[1][:, None, :]
        pk = pauli_k[None, :, :]
        src_k = jnp.stack([pk * (gi_r * gj_r - gi_i * gj_i), pk * (gi_r * gj_i + gi_i * gj_r)])
        lad_kb = lad_k[None, :, :]

        def left_mul(x):
            shp = x.shape
            flat = x.reshape(2 * shp[1], shp[2], shp[3])
            out = jnp.einsum("ab,bmn->amn", h_big, flat, precision=matmul_precision)
            return out.reshape(shp)

        def apply_ij(x):
            xr = x[0]
            xi = x[1]

            def li(hm, xm):
                return jnp.einsum("ia,kaj->kij", hm, xm, precision=matmul_precision)

            def lj(xm, hm):
                return jnp.einsum("kia,ja->kij", xm, hm, precision=matmul_precision)

            out_re = li(hre, xr) - li(him, xi) + lj(xr, hre) - lj(xi, him)
            out_im = li(hre, xi) + li(him, xr) + lj(xi, hre) + lj(xr, him)
            return jnp.stack([out_re, out_im])

        def to_k(x):
            xs = x.reshape(2, ndev, kb, nrows, ncols)
            got = lax.all_to_all(xs, ("row", "col"), 1, 1, tiled=True)
            rows = [
                jnp.concatenate([got[:, a * ncol + b] for b in range(ncol)], axis=-1)
                for a in range(nrow)
            ]
            return jnp.concatenate(rows, axis=-2)

        def send_k(y):
            return jnp.stack(
                [
                    y[:, :, a * nrows:(a + 1) * nrows, b * ncols:(b + 1) * ncols]
                    for a in range(nrow)
                    for b in range(ncol)
                ],
                axis=1,
            )

        def recv_k(ys):
            got = lax.all_to_all(ys, ("row", "col"), 1, 1, tiled=True)
            return got.reshape(2, orbs, nrows, ncols)

        dt = time_step
        dt2 = 0.5 * time_step * time_step
        g = green
        g_k = to_k(g)
        p = left_mul(g)
        p_got = lax.all_to_all(p.reshape(2, ndev, kb, nrows, ncols), ("row", "col"), 1, 1, tiled=True)
        q = apply_ij(g_k) + lad_kb * g_k

        def pblk(a, b):
            return p_got[:, a * ncol + b]

        def sub(x, a, b):
            return x[..., a * nrows:(a + 1) * nrows, b * ncols:(b + 1) * ncols]

        def e_blk(a, b):
            return pblk(a, b) + sub(q, a, b) + sub(src_k, a, b)

        def assemble(f):
            rows = [jnp.concatenate([f(a, b) for b in range(ncol)], axis=-1) for a in range(nrow)]
            return jnp.concatenate(rows, axis=-2)

        e = assemble(e_blk)
        w = assemble(lambda a, b: e_blk(a, b) + pblk(a, b))
        aw = apply_ij(w)

        def blk(x, a, b):
            return x[..., a * nrows:(a + 1) * nrows, b * ncols:(b + 1) * ncols]

        blocks = [
            neg_i(blk(q, a, b), dt) - dt2 * (blk(aw, a, b) + blk(lad_kb, a, b) * blk(e, a, b))
            for a in range(nrow)
            for b in range(ncol)
        ]
        ys, g2, p2 = lax.optimization_barrier((jnp.stack(blocks, axis=1), g, p))
        part_k_a = recv_k(ys)
        e2 = p2 + lad_a * g2 + src_a
        part_a = g2 + neg_i(p2 + src_a, dt) - dt2 * left_mul(e2)
        part_a = lax.optimization_barrier(with_layout_constraint(part_a, Layout((0, 1, 2, 3))))
        return part_a + part_k_a

    return on_device


def solution(mesh):
    placed = (
        P("grp", None, "row", "col"),
        P("grp", None, None),
        P("grp", None, None),
        P(),
        P(),
        P(),
        P(),
    )
    return jax.shard_map(
        make_on_device(mesh.shape["row"], mesh.shape["col"]),
        mesh=mesh,
        in_specs=placed,
        out_specs=P("grp", None, "row", "col"),
        check_vma=False,
    )
```

```python
import jax
import jax.numpy as jnp
from jax import lax
from jax.sharding import PartitionSpec as P
from jax.experimental.layout import Layout, with_layout_constraint

time_step = 0.1
matmul_precision = lax.Precision.HIGH


def neg_i(x, scale):
    return jnp.stack([scale * x[1], -scale * x[0]])


def make_on_device(nrow, ncol):
    ndev = nrow * ncol

    def on_device(green, hamiltonian, onebody, site_map, onsite_u, pair_first, pair_second):
        orbs = green.shape[1]
        nrows = green.shape[2]
        ncols = green.shape[3]
        kb = orbs // ndev
        r = lax.axis_index("row")
        c = lax.axis_index("col")
        row_start = r * nrows
        col_start = c * ncols
        k_start = (r * ncol + c) * kb
        levels = jnp.arange(onsite_u.shape[0], dtype=jnp.int32)
        orb_ids = jnp.arange(orbs, dtype=jnp.int32)
        u_all = jnp.sum(jnp.where(site_map[:, None] == levels[None, :], onsite_u[None, :], 0.0), axis=1)
        first_hot = (pair_first[:, None] == orb_ids[None, :]).astype(jnp.float32)
        second_hot = (pair_second[:, None] == orb_ids[None, :]).astype(jnp.float32)
        hre = hamiltonian[0]
        him = hamiltonian[1]
        h_big = jnp.concatenate(
            [jnp.concatenate([hre, -him], axis=1), jnp.concatenate([him, hre], axis=1)], axis=0
        )

        sites_i = lax.dynamic_slice_in_dim(site_map, row_start, nrows)
        sites_j = lax.dynamic_slice_in_dim(site_map, col_start, ncols)
        u_i = lax.dynamic_slice_in_dim(u_all, row_start, nrows)
        lad_a = u_i[:, None] * (sites_i[:, None] == sites_j[None, :]).astype(jnp.float32)
        fh_a = lax.dynamic_slice_in_dim(first_hot, row_start, nrows, 1)
        sh_a = lax.dynamic_slice_in_dim(second_hot, col_start, ncols, 1)
        pauli_a = u_i[:, None] * jnp.einsum("pi,pj->ij", fh_a, sh_a, precision=matmul_precision)
        left = lax.dynamic_slice_in_dim(onebody, row_start, nrows, 2)
        right = lax.dynamic_slice_in_dim(onebody, col_start, ncols, 2)
        src_a = jnp.stack([
            pauli_a * (left[0][:, :, None] * right[0][:, None, :] - left[1][:, :, None] * right[1][:, None, :]),
            pauli_a * (left[0][:, :, None] * right[1][:, None, :] + left[1][:, :, None] * right[0][:, None, :]),
        ])

        lad_k = u_all[:, None] * (site_map[:, None] == site_map[None, :]).astype(jnp.float32)
        pauli_k = u_all[:, None] * jnp.einsum("pi,pj->ij", first_hot, second_hot, precision=matmul_precision)
        gk = lax.dynamic_slice_in_dim(onebody, k_start, kb, 1)
        gi_r = gk[0][:, :, None]
        gi_i = gk[1][:, :, None]
        gj_r = gk[0][:, None, :]
        gj_i = gk[1][:, None, :]
        pk = pauli_k[None, :, :]
        src_k = jnp.stack([pk * (gi_r * gj_r - gi_i * gj_i), pk * (gi_r * gj_i + gi_i * gj_r)])
        lad_kb = lad_k[None, :, :]

        def left_mul(x):
            shp = x.shape
            flat = x.reshape(2 * shp[1], shp[2], shp[3])
            out = jnp.einsum("ab,bmn->amn", h_big, flat, precision=matmul_precision)
            return out.reshape(shp)

        def apply_ij(x):
            xr = x[0]
            xi = x[1]

            def li(hm, xm):
                return jnp.einsum("ia,kaj->kij", hm, xm, precision=matmul_precision)

            def lj(xm, hm):
                return jnp.einsum("kia,ja->kij", xm, hm, precision=matmul_precision)

            out_re = li(hre, xr) - li(him, xi) + lj(xr, hre) - lj(xi, him)
            out_im = li(hre, xi) + li(him, xr) + lj(xi, hre) + lj(xr, him)
            return jnp.stack([out_re, out_im])

        def to_k(x):
            xs = x.reshape(2, ndev, kb, nrows, ncols)
            got = lax.all_to_all(xs, ("row", "col"), 1, 1, tiled=True)
            rows = [
                jnp.concatenate([got[:, a * ncol + b] for b in range(ncol)], axis=-1)
                for a in range(nrow)
            ]
            return jnp.concatenate(rows, axis=-2)

        def send_k(y):
            return jnp.stack(
                [
                    y[:, :, a * nrows:(a + 1) * nrows, b * ncols:(b + 1) * ncols]
                    for a in range(nrow)
                    for b in range(ncol)
                ],
                axis=1,
            )

        dt = time_step
        dt2 = 0.5 * time_step * time_step
        g = green
        g_k = to_k(g)
        p = left_mul(g)
        p_got = lax.all_to_all(p.reshape(2, ndev, kb, nrows, ncols), ("row", "col"), 1, 1, tiled=True)
        q = apply_ij(g_k) + lad_kb * g_k

        def pblk(a, b):
            return p_got[:, a * ncol + b]

        def sub(x, a, b):
            return x[..., a * nrows:(a + 1) * nrows, b * ncols:(b + 1) * ncols]

        def e_blk(a, b):
            return pblk(a, b) + sub(q, a, b) + sub(src_k, a, b)

        def assemble(f):
            rows = [jnp.concatenate([f(a, b) for b in range(ncol)], axis=-1) for a in range(nrow)]
            return jnp.concatenate(rows, axis=-2)

        e = assemble(e_blk)
        w = assemble(lambda a, b: e_blk(a, b) + pblk(a, b))
        aw = apply_ij(w)

        def blk(x, a, b):
            return x[..., a * nrows:(a + 1) * nrows, b * ncols:(b + 1) * ncols]

        blocks = [
            neg_i(blk(q, a, b), dt) - dt2 * (blk(aw, a, b) + blk(lad_kb, a, b) * blk(e, a, b))
            for a in range(nrow)
            for b in range(ncol)
        ]
        ys, g2, p2 = lax.optimization_barrier((jnp.stack(blocks, axis=1), g, p))
        back = lax.all_to_all(ys, ("row", "col"), 1, 1, tiled=True)
        e2 = p2 + lad_a * g2 + src_a
        part_a = g2 + neg_i(p2 + src_a, dt) - dt2 * left_mul(e2)
        part_a = lax.optimization_barrier(with_layout_constraint(part_a, Layout((0, 1, 2, 3))))
        return jnp.concatenate(
            [part_a[:, d * kb:(d + 1) * kb] + back[:, d] for d in range(ndev)], axis=1
        )

    return on_device


def solution(mesh):
    placed = (
        P("grp", None, "row", "col"),
        P("grp", None, None),
        P("grp", None, None),
        P(),
        P(),
        P(),
        P(),
    )
    return jax.shard_map(
        make_on_device(mesh.shape["row"], mesh.shape["col"]),
        mesh=mesh,
        in_specs=placed,
        out_specs=P("grp", None, "row", "col"),
        check_vma=False,
    )
```

```python
import jax
import jax.numpy as jnp
from jax import lax
from jax.sharding import PartitionSpec as P
from jax.experimental.layout import Layout, with_layout_constraint

time_step = 0.1
matmul_precision = lax.Precision.HIGH


def neg_i(x, scale):
    return jnp.stack([scale * x[1], -scale * x[0]])


def make_on_device(nrow, ncol):
    ndev = nrow * ncol

    def on_device(green, hamiltonian, onebody, site_map, onsite_u, pair_first, pair_second):
        orbs = green.shape[1]
        nrows = green.shape[2]
        ncols = green.shape[3]
        kb = orbs // ndev
        r = lax.axis_index("row")
        c = lax.axis_index("col")
        row_start = r * nrows
        col_start = c * ncols
        k_start = (r * ncol + c) * kb
        levels = jnp.arange(onsite_u.shape[0], dtype=jnp.int32)
        orb_ids = jnp.arange(orbs, dtype=jnp.int32)
        u_all = jnp.sum(jnp.where(site_map[:, None] == levels[None, :], onsite_u[None, :], 0.0), axis=1)
        first_hot = (pair_first[:, None] == orb_ids[None, :]).astype(jnp.float32)
        second_hot = (pair_second[:, None] == orb_ids[None, :]).astype(jnp.float32)
        hre = hamiltonian[0]
        him = hamiltonian[1]
        h_big = jnp.concatenate(
            [jnp.concatenate([hre, -him], axis=1), jnp.concatenate([him, hre], axis=1)], axis=0
        )

        sites_i = lax.dynamic_slice_in_dim(site_map, row_start, nrows)
        sites_j = lax.dynamic_slice_in_dim(site_map, col_start, ncols)
        u_i = lax.dynamic_slice_in_dim(u_all, row_start, nrows)
        lad_a = u_i[:, None] * (sites_i[:, None] == sites_j[None, :]).astype(jnp.float32)
        fh_a = lax.dynamic_slice_in_dim(first_hot, row_start, nrows, 1)
        sh_a = lax.dynamic_slice_in_dim(second_hot, col_start, ncols, 1)
        pauli_a = u_i[:, None] * jnp.einsum("pi,pj->ij", fh_a, sh_a, precision=matmul_precision)
        left = lax.dynamic_slice_in_dim(onebody, row_start, nrows, 2)
        right = lax.dynamic_slice_in_dim(onebody, col_start, ncols, 2)
        src_a = jnp.stack([
            pauli_a * (left[0][:, :, None] * right[0][:, None, :] - left[1][:, :, None] * right[1][:, None, :]),
            pauli_a * (left[0][:, :, None] * right[1][:, None, :] + left[1][:, :, None] * right[0][:, None, :]),
        ])

        lad_k = u_all[:, None] * (site_map[:, None] == site_map[None, :]).astype(jnp.float32)
        pauli_k = u_all[:, None] * jnp.einsum("pi,pj->ij", first_hot, second_hot, precision=matmul_precision)
        gk = lax.dynamic_slice_in_dim(onebody, k_start, kb, 1)
        gi_r = gk[0][:, :, None]
        gi_i = gk[1][:, :, None]
        gj_r = gk[0][:, None, :]
        gj_i = gk[1][:, None, :]
        pk = pauli_k[None, :, :]
        src_k = jnp.stack([pk * (gi_r * gj_r - gi_i * gj_i), pk * (gi_r * gj_i + gi_i * gj_r)])
        lad_kb = lad_k[None, :, :]

        def left_mul(x):
            shp = x.shape
            flat = x.reshape(2 * shp[1], shp[2], shp[3])
            out = jnp.einsum("ab,bmn->amn", h_big, flat, precision=matmul_precision)
            return out.reshape(shp)

        def apply_ij(x):
            xr = x[0]
            xi = x[1]

            def li(hm, xm):
                return jnp.einsum("ia,kaj->kij", hm, xm, precision=matmul_precision)

            def lj(xm, hm):
                return jnp.einsum("kia,ja->kij", xm, hm, precision=matmul_precision)

            out_re = li(hre, xr) - li(him, xi) + lj(xr, hre) - lj(xi, him)
            out_im = li(hre, xi) + li(him, xr) + lj(xi, hre) + lj(xr, him)
            return jnp.stack([out_re, out_im])

        def to_k(x):
            xs = x.reshape(2, ndev, kb, nrows, ncols)
            got = lax.all_to_all(xs, ("row", "col"), 1, 1, tiled=True)
            rows = [
                jnp.concatenate([got[:, a * ncol + b] for b in range(ncol)], axis=-1)
                for a in range(nrow)
            ]
            return jnp.concatenate(rows, axis=-2)

        def send_k(y):
            return jnp.stack(
                [
                    y[:, :, a * nrows:(a + 1) * nrows, b * ncols:(b + 1) * ncols]
                    for a in range(nrow)
                    for b in range(ncol)
                ],
                axis=1,
            )

        def recv_k(ys):
            got = lax.all_to_all(ys, ("row", "col"), 1, 1, tiled=True)
            return got.reshape(2, orbs, nrows, ncols)

        dt = time_step
        dt2 = 0.5 * time_step * time_step
        g = green
        g_k = to_k(g)
        p = left_mul(g)
        p_got = lax.all_to_all(p.reshape(2, ndev, kb, nrows, ncols), ("row", "col"), 1, 1, tiled=True)
        q = apply_ij(g_k) + lad_kb * g_k

        def pblk(a, b):
            return p_got[:, a * ncol + b]

        def sub(x, a, b):
            return x[..., a * nrows:(a + 1) * nrows, b * ncols:(b + 1) * ncols]

        def e_blk(a, b):
            return pblk(a, b) + sub(q, a, b) + sub(src_k, a, b)

        def assemble(f):
            rows = [jnp.concatenate([f(a, b) for b in range(ncol)], axis=-1) for a in range(nrow)]
            return jnp.concatenate(rows, axis=-2)

        e = assemble(e_blk)
        pre = apply_ij(q + src_k)
        p2k = assemble(lambda a, b: pblk(a, b) + pblk(a, b))
        aw = apply_ij(p2k) + pre

        def blk(x, a, b):
            return x[..., a * nrows:(a + 1) * nrows, b * ncols:(b + 1) * ncols]

        blocks = [
            neg_i(blk(q, a, b), dt) - dt2 * (blk(aw, a, b) + blk(lad_kb, a, b) * blk(e, a, b))
            for a in range(nrow)
            for b in range(ncol)
        ]
        ys, g2, p2 = lax.optimization_barrier((jnp.stack(blocks, axis=1), g, p))
        part_k_a = recv_k(ys)
        e2 = p2 + lad_a * g2 + src_a
        part_a = g2 + neg_i(p2 + src_a, dt) - dt2 * left_mul(e2)
        part_a = lax.optimization_barrier(with_layout_constraint(part_a, Layout((0, 1, 2, 3))))
        return part_a + part_k_a

    return on_device


def solution(mesh):
    placed = (
        P("grp", None, "row", "col"),
        P("grp", None, None),
        P("grp", None, None),
        P(),
        P(),
        P(),
        P(),
    )
    return jax.shard_map(
        make_on_device(mesh.shape["row"], mesh.shape["col"]),
        mesh=mesh,
        in_specs=placed,
        out_specs=P("grp", None, "row", "col"),
        check_vma=False,
    )
```
